256 devices in a mesh: expert: 32 (over z, x), helper: 8 (over y, core).
Axes of the slice: x: 4, y: 4, z: 8, core: 2. Of those that a mesh axis runs over, the one named last changes fastest.
Arguments:
- route_ids: int32 [65536], P(('expert', 'helper')), may hold values from 0 to 255, as said below
- hot_expert: int32 [256], replicated, may hold values from 0 to 255, as said below
- features: bfloat16 [65536, 1024], P(('expert', 'helper')), may hold values from -6 to 6
- tangents: bfloat16 [3, 65536, 1024], P(None, ('expert', 'helper')), may hold values from -6 to 6
- expert_weight: bfloat16 [256, 1024, 1024], P(('expert', 'helper')), may hold values from -0.1875 to 0.1875
- expert_bias: bfloat16 [256, 1024], P(('expert', 'helper')), may hold values from -3 to 3
- cot_value: bfloat16 [65536, 1024], P(('expert', 'helper')), may hold values from -0.375 to 0.375
- cot_tangent: bfloat16 [3, 65536, 1024], P(None, ('expert', 'helper')), may hold values from -0.375 to 0.375
Outputs:
- value_out: bfloat16 [65536, 1024], P(('expert', 'helper'))
- tangent_out: bfloat16 [3, 65536, 1024], P(None, ('expert', 'helper'))
- grad_weight: bfloat16 [256, 1024, 1024], P(('expert', 'helper'))
- grad_bias: float32 [256, 1024], P(('expert', 'helper'))
The draws below stay inside these ranges and needn't reach their ends.
Inputs may be any that keep to these rules, and one draw needn't show every extreme that they name: `route_ids`: among the 256 points of each device, the expert hot_expert[0] is named 3 times; a quarter of the experts less one are named 2 times each, half of the experts less one are named once each, the rest never. `hot_expert`: each expert appears once; the first entry is the expert that every device names 3 times.
All inputs are finite; a program needn't handle non-finite values.
Results may differ from the reference program's by a relative error of at most 0.0049.
Values may be sent and summed in bfloat16 or wider, within the bound.
No kernel may reach another device: no remote copies, remote signals or barrier semaphores. Data moves between devices by JAX's collectives and lax.ppermute only.
A program may use at most 192 MiB of HBM per device.

```python
import jax
import jax.numpy as jnp
from jax import lax

D = 1024
ROWS_DEV = 256
EXPERTS = 256
TOKENS = 65536
CAP = 2


def replica_table(key):
    return jax.random.permutation(jax.random.fold_in(key, 11), EXPERTS).astype(jnp.int32)


def pick_hot(key):
    return replica_table(key)[0].astype(jnp.int32)


def draw_hot_expert(key, part):
    return replica_table(key).reshape(EXPERTS).astype(jnp.int32)


def draw_route_ids(key, part):
    hottest = pick_hot(key)
    device_keys = jax.random.split(jax.random.fold_in(key, 13), EXPERTS)
    hot_rows = 3 * CAP // 2
    halfway = hot_rows + (EXPERTS // 4 - 1) * CAP

    def one_device(device_key):
        key_perm, key_order = jax.random.split(device_key)
        ranking = jax.random.permutation(key_perm, EXPERTS).astype(jnp.int32)
        found = jnp.argmax(ranking == hottest).astype(jnp.int32)
        ranking = ranking.at[found].set(ranking[0]).at[0].set(hottest)
        sample_index = jnp.arange(ROWS_DEV, dtype=jnp.int32)
        middle = 1 + (sample_index - hot_rows) // CAP
        tail = EXPERTS // 4 + (sample_index - halfway) // (CAP // 2)
        position = jnp.where(sample_index < hot_rows, 0, jnp.where(sample_index < halfway, middle, tail)).astype(jnp.int32)
        targets = ranking[position]
        shuffle = jax.random.permutation(key_order, ROWS_DEV).astype(jnp.int32)
        return targets[shuffle]
    return jax.vmap(one_device)(device_keys).reshape(TOKENS).astype(jnp.int32)


def block_scale(key, dims, cuts, smallest, largest):
    def one(dim, parts):
        draws = jax.random.uniform(jax.random.fold_in(jax.random.fold_in(key, 6), dim), (parts,), jnp.float32, smallest / len(cuts), largest / len(cuts))
        return jnp.repeat(jnp.exp(draws), dims[dim] // parts).reshape((-1,) + (1,) * (len(dims) - dim - 1))

    gain = one(*cuts[0])
    for cut in cuts[1:]:
        gain = gain * one(*cut)
    return gain


def scatter_about(stream_key, extent, deviation, most, shards=(), kind=jnp.bfloat16):
    result = deviation * jax.random.normal(stream_key, extent, jnp.float32)
    if shards:
        result = result * block_scale(stream_key, extent, shards, -0.22, 0.18)
    return jnp.clip(result, -most, most).astype(kind)


def setup_inputs(seed: int = 0) -> dict:
    key_of = jax.random.split(jax.random.key(seed), 9)
    return {
        "route_ids": draw_route_ids(jax.random.fold_in(key_of[8], 71), 0),
        "hot_expert": draw_hot_expert(jax.random.fold_in(key_of[8], 71), 0),
        "features": scatter_about(key_of[2], (TOKENS, D), 1.0, 6.0, ((0, 256),)),
        "tangents": scatter_about(key_of[3], (3, TOKENS, D), 1.0, 6.0, ((1, 256),)),
        "expert_weight": scatter_about(key_of[4], (EXPERTS, D, D), D ** -0.5, 0.1875, ((0, 256),)),
        "expert_bias": scatter_about(key_of[5], (EXPERTS, D), 0.5, 3.0, ((0, 256),)),
        "cot_value": scatter_about(key_of[6], (TOKENS, D), 0.0625, 0.375, ((0, 256),)),
        "cot_tangent": scatter_about(key_of[7], (3, TOKENS, D), 0.0625, 0.375, ((1, 256),)),
    }


def expert_pass(inputs, weight, bias_row, cotangent):
    slot_count = inputs.shape[1]
    feature_dim = inputs.shape[2]
    flattened = inputs.reshape(4 * slot_count, feature_dim)
    product = jnp.dot(flattened, weight, preferred_element_type=jnp.float32).reshape(4, slot_count, feature_dim)
    preact = product[0] + bias_row[None, :]
    directed = product[1:]
    slopes = jax.nn.sigmoid(preact)
    values = jax.nn.softplus(preact).astype(jnp.bfloat16)
    carried = (slopes[None] * directed).astype(jnp.bfloat16)
    results = jnp.concatenate([values[None], carried], axis=0)
    cot_float = cotangent.astype(jnp.float32)
    grad_pre = cot_float[0] * slopes + jnp.sum(cot_float[1:] * directed, axis=0) * slopes * (1.0 - slopes)
    grad_dir = (cot_float[1:] * slopes[None]).astype(jnp.bfloat16)
    gradients = jnp.concatenate([grad_pre.astype(jnp.bfloat16)[None], grad_dir], axis=0).reshape(4 * slot_count, feature_dim)
    weight_grad = jnp.dot(flattened.T, gradients, preferred_element_type=jnp.float32)
    bias_grad = jnp.sum(grad_pre, axis=0)
    return results, weight_grad, bias_grad


def reference(route_ids, hot_expert, features, tangents, expert_weight, expert_bias, cot_value, cot_tangent):
    hot_id = hot_expert[0]
    counts = jnp.zeros((EXPERTS,), jnp.int32).at[route_ids].add(1)
    starts = (jnp.cumsum(counts) - counts).astype(jnp.int32)
    ordering = jnp.argsort(route_ids, stable=True).astype(jnp.int32)
    width_slots = EXPERTS * CAP

    def segment(expert, offset):
        lane_index = jnp.arange(width_slots, dtype=jnp.int32)
        rank_slot = (offset + lane_index).astype(jnp.int32)
        position = jnp.clip(starts[expert] + rank_slot, 0, TOKENS - 1).astype(jnp.int32)
        samples = jnp.where(rank_slot < counts[expert], ordering[position], TOKENS).astype(jnp.int32)
        leading = jnp.take(features, samples, axis=0, mode="fill", fill_value=0)
        others = jnp.take(tangents, samples, axis=1, mode="fill", fill_value=0)
        inputs = jnp.concatenate([leading[None], others], axis=0)
        cot_lead = jnp.take(cot_value, samples, axis=0, mode="fill", fill_value=0)
        cot_others = jnp.take(cot_tangent, samples, axis=1, mode="fill", fill_value=0)
        cotangent = jnp.concatenate([cot_lead[None], cot_others], axis=0)
        results, seg_weight, seg_bias = expert_pass(inputs, expert_weight[expert], expert_bias[expert], cotangent)
        return samples, results, seg_weight, seg_bias

    def one_expert(expert, carried):
        outputs, grad_w, grad_b, hot_w, hot_b = carried
        samples, results, seg_weight, seg_bias = segment(expert, jnp.int32(0))
        outputs = outputs.at[:, samples].set(results, mode="drop")
        grad_w = grad_w.at[expert].set(seg_weight.astype(jnp.bfloat16))
        grad_b = grad_b.at[expert].set(seg_bias)
        is_hot = expert == hot_id
        hot_w = jnp.where(is_hot, seg_weight, hot_w)
        hot_b = jnp.where(is_hot, seg_bias, hot_b)
        return outputs, grad_w, grad_b, hot_w, hot_b

    initial = (jnp.zeros((4, TOKENS, D), jnp.bfloat16), jnp.zeros((EXPERTS, D, D), jnp.bfloat16), jnp.zeros((EXPERTS, D), jnp.float32), jnp.zeros((D, D), jnp.float32), jnp.zeros((D,), jnp.float32))
    outputs, grad_w, grad_b, hot_w, hot_b = lax.fori_loop(0, EXPERTS, one_expert, initial)
    samples, results, seg_weight, seg_bias = segment(hot_id, jnp.int32(width_slots))
    outputs = outputs.at[:, samples].set(results, mode="drop")
    grad_w = grad_w.at[hot_id].set((hot_w + seg_weight).astype(jnp.bfloat16))
    grad_b = grad_b.at[hot_id].set(hot_b + seg_bias)
    return outputs[0], outputs[1:], grad_w, grad_b
```

```python
import jax
import jax.numpy as jnp
from jax import lax
from jax.sharding import PartitionSpec as P

AXES = ("expert", "helper")


def lower_ones(samples):
    index = jnp.arange(samples, dtype=jnp.int32)
    return (index[:, None] > index[None, :]).astype(jnp.bfloat16)


def ranks_of(route_ids, groups):
    samples = route_ids.shape[0]
    onehot = (route_ids[:, None] == jnp.arange(groups, dtype=jnp.int32)[None, :]).astype(
        jnp.bfloat16
    )
    before = jnp.dot(lower_ones(samples), onehot, preferred_element_type=jnp.float32)
    return jnp.sum(before * onehot.astype(jnp.float32), axis=1).astype(jnp.int32)


def expert_pass(inputs, cotangent, weight, bias_row):
    slot_count, depth, feature_dim = inputs.shape
    flat = inputs.reshape(slot_count * depth, feature_dim)
    product = jnp.dot(flat, weight, preferred_element_type=jnp.float32).reshape(
        slot_count, depth, feature_dim
    )
    preact = product[:, 0] + bias_row[None, :]
    directed = product[:, 1:]
    slopes = jax.nn.sigmoid(preact)
    values = jax.nn.softplus(preact).astype(jnp.bfloat16)
    carried = (slopes[:, None] * directed).astype(jnp.bfloat16)
    results = jnp.concatenate([values[:, None], carried], axis=1)
    cot_float = cotangent.astype(jnp.float32)
    grad_pre = cot_float[:, 0] * slopes + jnp.sum(cot_float[:, 1:] * directed, axis=1) * slopes * (
        1.0 - slopes
    )
    grad_dir = (cot_float[:, 1:] * slopes[:, None]).astype(jnp.bfloat16)
    gradients = jnp.concatenate([grad_pre.astype(jnp.bfloat16)[:, None], grad_dir], axis=1)
    weight_grad = lax.dot_general(
        flat,
        gradients.reshape(slot_count * depth, feature_dim),
        (((0,), (0,)), ((), ())),
        preferred_element_type=jnp.float32,
    )
    return results, weight_grad, jnp.sum(grad_pre, axis=0)


def body(
    route_ids, hot_expert, features, tangents, expert_weight, expert_bias, cot_value, cot_tangent
):
    n_expert = lax.axis_size("expert")
    n_helper = lax.axis_size("helper")
    groups = n_expert * n_helper
    samples = route_ids.shape[0]
    feature_dim = features.shape[1]
    cap = 2 * samples // groups
    me = lax.axis_index("expert") * n_helper + lax.axis_index("helper")
    is_hot = me == hot_expert[0]

    rank = ranks_of(route_ids, groups)
    slot = route_ids * cap + rank
    main = rank < cap
    dispatch = (
        (slot[None, :] == jnp.arange(groups * cap, dtype=jnp.int32)[:, None]) & main[None, :]
    ).astype(jnp.bfloat16)
    extra = jnp.logical_not(main)

    stacked = jnp.concatenate([features[None], tangents, cot_value[None], cot_tangent], axis=0)
    send = jnp.einsum(
        "sp,apd->sad", dispatch, stacked, preferred_element_type=jnp.float32
    ).astype(jnp.bfloat16)
    extra_rows = jnp.einsum(
        "p,apd->ad", extra.astype(jnp.bfloat16), stacked, preferred_element_type=jnp.float32
    ).astype(jnp.bfloat16)

    gathered = lax.all_gather(extra_rows, AXES, axis=0, tiled=False)
    gathered = jnp.where(is_hot, gathered, jnp.zeros_like(gathered))
    received = lax.all_to_all(
        send.reshape(groups, cap * 8, feature_dim), AXES, 0, 0, tiled=True
    ).reshape(groups * cap, 8, feature_dim)

    weight = expert_weight[0]
    bias_row = expert_bias[0]
    results, weight_grad, bias_grad = expert_pass(
        received[:, :4], received[:, 4:], weight, bias_row
    )
    extra_results, extra_wg, extra_bg = expert_pass(
        gathered[:, :4], gathered[:, 4:], weight, bias_row
    )

    returned = lax.all_to_all(
        results.reshape(groups, cap * 4, feature_dim), AXES, 0, 0, tiled=True
    ).reshape(groups * cap, 4, feature_dim)
    extra_results = jnp.where(is_hot, extra_results, jnp.zeros_like(extra_results))
    extra_back = lax.psum_scatter(extra_results, AXES, scatter_dimension=0, tiled=True)[0]

    combined = jnp.einsum(
        "sp,sad->apd", dispatch, returned, preferred_element_type=jnp.float32
    ).astype(jnp.bfloat16)
    outputs = jnp.where(extra[None, :, None], extra_back[:, None, :], combined)
    grad_weight = (weight_grad + extra_wg).astype(jnp.bfloat16)[None]
    grad_bias = (bias_grad + extra_bg)[None]
    return (outputs[0], outputs[1:], grad_weight, grad_bias)


def solution(mesh):
    return jax.shard_map(
        body,
        mesh=mesh,
        in_specs=(
            P(("expert", "helper")),
            P(),
            P(("expert", "helper"), None),
            P(None, ("expert", "helper"), None),
            P(("expert", "helper"), None, None),
            P(("expert", "helper"), None),
            P(("expert", "helper"), None),
            P(None, ("expert", "helper"), None),
        ),
        out_specs=(
            P(("expert", "helper"), None),
            P(None, ("expert", "helper"), None),
            P(("expert", "helper"), None, None),
            P(("expert", "helper"), None),
        ),
        check_vma=False,
    )
```

```python
import jax
import jax.numpy as jnp
from jax import lax
from jax.sharding import PartitionSpec as P

AXES = ("expert", "helper")


def lower_ones(samples):
    index = jnp.arange(samples, dtype=jnp.int32)
    return (index[:, None] > index[None, :]).astype(jnp.bfloat16)


def ranks_of(route_ids, groups):
    samples = route_ids.shape[0]
    onehot = (route_ids[:, None] == jnp.arange(groups, dtype=jnp.int32)[None, :]).astype(
        jnp.bfloat16
    )
    before = jnp.dot(lower_ones(samples), onehot, preferred_element_type=jnp.float32)
    return jnp.sum(before * onehot.astype(jnp.float32), axis=1).astype(jnp.int32)


def expert_pass(inputs, cotangent, weight, bias_row):
    slot_count, depth, feature_dim = inputs.shape
    flat = inputs.reshape(slot_count * depth, feature_dim)
    product = jnp.dot(flat, weight, preferred_element_type=jnp.float32).reshape(
        slot_count, depth, feature_dim
    )
    preact = product[:, 0] + bias_row[None, :]
    directed = product[:, 1:]
    slopes = jax.nn.sigmoid(preact)
    values = jax.nn.softplus(preact).astype(jnp.bfloat16)
    carried = (slopes[:, None] * directed).astype(jnp.bfloat16)
    results = jnp.concatenate([values[:, None], carried], axis=1)
    cot_float = cotangent.astype(jnp.float32)
    grad_pre = cot_float[:, 0] * slopes + jnp.sum(cot_float[:, 1:] * directed, axis=1) * slopes * (
        1.0 - slopes
    )
    grad_dir = (cot_float[:, 1:] * slopes[:, None]).astype(jnp.bfloat16)
    gradients = jnp.concatenate([grad_pre.astype(jnp.bfloat16)[:, None], grad_dir], axis=1)
    weight_grad = lax.dot_general(
        flat,
        gradients.reshape(slot_count * depth, feature_dim),
        (((0,), (0,)), ((), ())),
        preferred_element_type=jnp.float32,
    )
    return results, weight_grad, jnp.sum(grad_pre, axis=0)


def body(
    route_ids, hot_expert, features, tangents, expert_weight, expert_bias, cot_value, cot_tangent
):
    n_expert = lax.axis_size("expert")
    n_helper = lax.axis_size("helper")
    groups = n_expert * n_helper
    samples = route_ids.shape[0]
    feature_dim = features.shape[1]
    cap = 2 * samples // groups
    me = lax.axis_index("expert") * n_helper + lax.axis_index("helper")
    is_hot = me == hot_expert[0]

    rank = ranks_of(route_ids, groups)
    slot = route_ids * cap + rank
    main = rank < cap
    dispatch = (
        (slot[None, :] == jnp.arange(groups * cap, dtype=jnp.int32)[:, None]) & main[None, :]
    ).astype(jnp.bfloat16)
    extra = jnp.logical_not(main)

    stacked = jnp.concatenate(
        [features[:, None], tangents.transpose(1, 0, 2), cot_value[:, None], cot_tangent.transpose(1, 0, 2)],
        axis=1,
    ).reshape(samples, 8 * feature_dim)
    send = jnp.dot(dispatch, stacked, preferred_element_type=jnp.float32).astype(jnp.bfloat16)
    extra_rows = jnp.dot(
        extra.astype(jnp.bfloat16)[None, :], stacked, preferred_element_type=jnp.float32
    ).astype(jnp.bfloat16)

    gathered = lax.all_gather(extra_rows.reshape(8, feature_dim), AXES, axis=0, tiled=False)
    gathered = jnp.where(is_hot, gathered, jnp.zeros_like(gathered))
    received = lax.all_to_all(
        send.reshape(groups, cap * 8, feature_dim), AXES, 0, 0, tiled=True
    ).reshape(groups * cap, 8, feature_dim)

    weight = expert_weight[0]
    bias_row = expert_bias[0]
    results, weight_grad, bias_grad = expert_pass(
        received[:, :4], received[:, 4:], weight, bias_row
    )
    extra_results, extra_wg, extra_bg = expert_pass(
        gathered[:, :4], gathered[:, 4:], weight, bias_row
    )

    back = jnp.concatenate(
        [results.reshape(groups, cap, 4, feature_dim), extra_results[:, None]], axis=1
    ).reshape(groups, (cap + 1) * 4, feature_dim)
    returned = lax.all_to_all(back, AXES, 0, 0, tiled=True).reshape(groups, cap + 1, 4, feature_dim)
    extra_back = lax.dynamic_index_in_dim(returned[:, cap], hot_expert[0], axis=0, keepdims=False)

    combined = jnp.einsum(
        "sp,sad->apd",
        dispatch,
        returned[:, :cap].reshape(groups * cap, 4, feature_dim),
        preferred_element_type=jnp.float32,
    ).astype(jnp.bfloat16)
    outputs = jnp.where(extra[None, :, None], extra_back[:, None, :], combined)
    grad_weight = (weight_grad + extra_wg).astype(jnp.bfloat16)[None]
    grad_bias = (bias_grad + extra_bg)[None]
    return (outputs[0], outputs[1:], grad_weight, grad_bias)


def solution(mesh):
    return jax.shard_map(
        body,
        mesh=mesh,
        in_specs=(
            P(("expert", "helper")),
            P(),
            P(("expert", "helper"), None),
            P(None, ("expert", "helper"), None),
            P(("expert", "helper"), None, None),
            P(("expert", "helper"), None),
            P(("expert", "helper"), None),
            P(None, ("expert", "helper"), None),
        ),
        out_specs=(
            P(("expert", "helper"), None),
            P(None, ("expert", "helper"), None),
            P(("expert", "helper"), None, None),
            P(("expert", "helper"), None),
        ),
        check_vma=False,
    )
```

```python
import jax
import jax.numpy as jnp
from jax import lax
from jax.sharding import PartitionSpec as P

AXES = ("expert", "helper")


def lower_ones(samples):
    index = jnp.arange(samples, dtype=jnp.int32)
    return (index[:, None] > index[None, :]).astype(jnp.bfloat16)


def ranks_of(route_ids, groups):
    samples = route_ids.shape[0]
    onehot = (route_ids[:, None] == jnp.arange(groups, dtype=jnp.int32)[None, :]).astype(
        jnp.bfloat16
    )
    before = jnp.dot(lower_ones(samples), onehot, preferred_element_type=jnp.float32)
    return jnp.sum(before * onehot.astype(jnp.float32), axis=1).astype(jnp.int32)


def expert_pass(inputs, cotangent, weight, bias_row):
    slot_count, depth, feature_dim = inputs.shape
    flat = inputs.reshape(slot_count * depth, feature_dim)
    product = jnp.dot(flat, weight, preferred_element_type=jnp.float32).reshape(
        slot_count, depth, feature_dim
    )
    preact = product[:, 0] + bias_row[None, :]
    directed = product[:, 1:]
    slopes = jax.nn.sigmoid(preact)
    values = jax.nn.softplus(preact).astype(jnp.bfloat16)
    carried = (slopes[:, None] * directed).astype(jnp.bfloat16)
    results = jnp.concatenate([values[:, None], carried], axis=1)
    cot_float = cotangent.astype(jnp.float32)
    grad_pre = cot_float[:, 0] * slopes + jnp.sum(cot_float[:, 1:] * directed, axis=1) * slopes * (
        1.0 - slopes
    )
    grad_dir = (cot_float[:, 1:] * slopes[:, None]).astype(jnp.bfloat16)
    gradients = jnp.concatenate([grad_pre.astype(jnp.bfloat16)[:, None], grad_dir], axis=1)
    weight_grad = lax.dot_general(
        flat,
        gradients.reshape(slot_count * depth, feature_dim),
        (((0,), (0,)), ((), ())),
        preferred_element_type=jnp.float32,
    )
    return results, weight_grad, jnp.sum(grad_pre, axis=0)


def body(
    route_ids, hot_expert, features, tangents, expert_weight, expert_bias, cot_value, cot_tangent
):
    n_expert = lax.axis_size("expert")
    n_helper = lax.axis_size("helper")
    groups = n_expert * n_helper
    samples = route_ids.shape[0]
    feature_dim = features.shape[1]
    cap = 2 * samples // groups
    me = lax.axis_index("expert") * n_helper + lax.axis_index("helper")
    is_hot = me == hot_expert[0]
    weight = expert_weight[0]
    bias_row = expert_bias[0]

    rank = ranks_of(route_ids, groups)
    to_expert = route_ids[None, :] == jnp.arange(groups, dtype=jnp.int32)[:, None]
    extra = rank >= cap
    stacked = jnp.concatenate([features[None], tangents, cot_value[None], cot_tangent], axis=0)

    dispatches = []
    sends = []
    for c in range(cap):
        dispatch = (to_expert & (rank == c)[None, :]).astype(jnp.bfloat16)
        dispatches.append(dispatch)
        sends.append(
            jnp.einsum(
                "sp,apd->sad", dispatch, stacked, preferred_element_type=jnp.float32
            ).astype(jnp.bfloat16)
        )
    extra_rows = jnp.einsum(
        "p,apd->ad", extra.astype(jnp.bfloat16), stacked, preferred_element_type=jnp.float32
    ).astype(jnp.bfloat16)
    gathered = lax.all_gather(extra_rows, AXES, axis=0, tiled=False)
    gathered = jnp.where(is_hot, gathered, jnp.zeros_like(gathered))

    extra_results, weight_grad, bias_grad = expert_pass(
        gathered[:, :4], gathered[:, 4:], weight, bias_row
    )
    returned = []
    for c in range(cap):
        received = lax.all_to_all(sends[c], AXES, 0, 0, tiled=True)
        results, slot_wg, slot_bg = expert_pass(received[:, :4], received[:, 4:], weight, bias_row)
        weight_grad = weight_grad + slot_wg
        bias_grad = bias_grad + slot_bg
        if c == 0:
            results = jnp.concatenate([results, extra_results], axis=1)
        returned.append(lax.all_to_all(results, AXES, 0, 0, tiled=True))

    extra_back = lax.dynamic_index_in_dim(returned[0][:, 4:], hot_expert[0], axis=0, keepdims=False)
    combined = jnp.einsum(
        "sp,sad->apd", dispatches[0], returned[0][:, :4], preferred_element_type=jnp.float32
    )
    for c in range(1, cap):
        combined = combined + jnp.einsum(
            "sp,sad->apd", dispatches[c], returned[c], preferred_element_type=jnp.float32
        )
    outputs = jnp.where(extra[None, :, None], extra_back[:, None, :], combined.astype(jnp.bfloat16))
    return (outputs[0], outputs[1:], weight_grad.astype(jnp.bfloat16)[None], bias_grad[None])


def solution(mesh):
    return jax.shard_map(
        body,
        mesh=mesh,
        in_specs=(
            P(("expert", "helper")),
            P(),
            P(("expert", "helper"), None),
            P(None, ("expert", "helper"), None),
            P(("expert", "helper"), None, None),
            P(("expert", "helper"), None),
            P(("expert", "helper"), None),
            P(None, ("expert", "helper"), None),
        ),
        out_specs=(
            P(("expert", "helper"), None),
            P(None, ("expert", "helper"), None),
            P(("expert", "helper"), None, None),
            P(("expert", "helper"), None),
        ),
        check_vma=False,
    )
```

```python
import jax
import jax.numpy as jnp
from jax import lax
from jax.sharding import PartitionSpec as P

AXES = ("expert", "helper")


def lower_ones(samples):
    index = jnp.arange(samples, dtype=jnp.int32)
    return (index[:, None] > index[None, :]).astype(jnp.bfloat16)


def ranks_of(route_ids, groups):
    samples = route_ids.shape[0]
    onehot = (route_ids[:, None] == jnp.arange(groups, dtype=jnp.int32)[None, :]).astype(
        jnp.bfloat16
    )
    before = jnp.dot(lower_ones(samples), onehot, preferred_element_type=jnp.float32)
    return jnp.sum(before * onehot.astype(jnp.float32), axis=1).astype(jnp.int32)


def forward_pass(inputs, weight, bias_row):
    slot_count, depth, feature_dim = inputs.shape
    product = jnp.dot(
        inputs.reshape(slot_count * depth, feature_dim), weight, preferred_element_type=jnp.float32
    ).reshape(slot_count, depth, feature_dim)
    preact = product[:, 0] + bias_row[None, :]
    directed = product[:, 1:]
    slopes = jax.nn.sigmoid(preact)
    values = jax.nn.softplus(preact).astype(jnp.bfloat16)
    carried = (slopes[:, None] * directed).astype(jnp.bfloat16)
    return jnp.concatenate([values[:, None], carried], axis=1), slopes, directed


def backward_pass(inputs, slopes, directed, cotangent):
    slot_count, depth, feature_dim = inputs.shape
    cot_float = cotangent.astype(jnp.float32)
    grad_pre = cot_float[:, 0] * slopes + jnp.sum(cot_float[:, 1:] * directed, axis=1) * slopes * (
        1.0 - slopes
    )
    grad_dir = (cot_float[:, 1:] * slopes[:, None]).astype(jnp.bfloat16)
    gradients = jnp.concatenate([grad_pre.astype(jnp.bfloat16)[:, None], grad_dir], axis=1)
    weight_grad = lax.dot_general(
        inputs.reshape(slot_count * depth, feature_dim),
        gradients.reshape(slot_count * depth, feature_dim),
        (((0,), (0,)), ((), ())),
        preferred_element_type=jnp.float32,
    )
    return weight_grad, jnp.sum(grad_pre, axis=0)


def body(
    route_ids, hot_expert, features, tangents, expert_weight, expert_bias, cot_value, cot_tangent
):
    n_expert = lax.axis_size("expert")
    n_helper = lax.axis_size("helper")
    groups = n_expert * n_helper
    samples = route_ids.shape[0]
    feature_dim = features.shape[1]
    cap = 2 * samples // groups
    me = lax.axis_index("expert") * n_helper + lax.axis_index("helper")
    is_hot = me == hot_expert[0]
    weight = expert_weight[0]
    bias_row = expert_bias[0]

    rank = ranks_of(route_ids, groups)
    slot = route_ids * cap + rank
    main = rank < cap
    dispatch = (
        (slot[None, :] == jnp.arange(groups * cap, dtype=jnp.int32)[:, None]) & main[None, :]
    ).astype(jnp.bfloat16)
    extra = jnp.logical_not(main)

    def place(stacked):
        return jnp.einsum(
            "sp,apd->sad", dispatch, stacked, preferred_element_type=jnp.float32
        ).astype(jnp.bfloat16).reshape(groups, cap * 4, feature_dim)

    def transfer(stacked):
        return lax.all_to_all(stacked, AXES, 0, 0, tiled=True).reshape(groups * cap, 4, feature_dim)

    inputs_local = jnp.concatenate([features[None], tangents], axis=0)
    cot_local = jnp.concatenate([cot_value[None], cot_tangent], axis=0)
    stacked = jnp.concatenate([inputs_local, cot_local], axis=0)
    extra_rows = jnp.einsum(
        "p,apd->ad", extra.astype(jnp.bfloat16), stacked, preferred_element_type=jnp.float32
    ).astype(jnp.bfloat16)
    gathered = lax.all_gather(extra_rows, AXES, axis=0, tiled=False)
    gathered = jnp.where(is_hot, gathered, jnp.zeros_like(gathered))

    inputs = transfer(place(inputs_local))
    inputs, cot_send = lax.optimization_barrier((inputs, place(cot_local)))
    cotangent = transfer(cot_send)

    results, slopes, directed = forward_pass(inputs, weight, bias_row)
    extra_results, extra_slopes, extra_directed = forward_pass(gathered[:, :4], weight, bias_row)
    back = jnp.concatenate(
        [results.reshape(groups, cap, 4, feature_dim), extra_results[:, None]], axis=1
    ).reshape(groups, (cap + 1) * 4, feature_dim)
    back, slopes, directed, extra_slopes, extra_directed = lax.optimization_barrier(
        (back, slopes, directed, extra_slopes, extra_directed)
    )
    returned = lax.all_to_all(back, AXES, 0, 0, tiled=True).reshape(groups, cap + 1, 4, feature_dim)

    weight_grad, bias_grad = backward_pass(inputs, slopes, directed, cotangent)
    extra_wg, extra_bg = backward_pass(gathered[:, :4], extra_slopes, extra_directed, gathered[:, 4:])

    extra_back = lax.dynamic_index_in_dim(returned[:, cap], hot_expert[0], axis=0, keepdims=False)
    combined = jnp.einsum(
        "sp,sad->apd",
        dispatch,
        returned[:, :cap].reshape(groups * cap, 4, feature_dim),
        preferred_element_type=jnp.float32,
    ).astype(jnp.bfloat16)
    outputs = jnp.where(extra[None, :, None], extra_back[:, None, :], combined)
    grad_weight = (weight_grad + extra_wg).astype(jnp.bfloat16)[None]
    grad_bias = (bias_grad + extra_bg)[None]
    return (outputs[0], outputs[1:], grad_weight, grad_bias)


def solution(mesh):
    return jax.shard_map(
        body,
        mesh=mesh,
        in_specs=(
            P(("expert", "helper")),
            P(),
            P(("expert", "helper"), None),
            P(None, ("expert", "helper"), None),
            P(("expert", "helper"), None, None),
            P(("expert", "helper"), None),
            P(("expert", "helper"), None),
            P(None, ("expert", "helper"), None),
        ),
        out_specs=(
            P(("expert", "helper"), None),
            P(None, ("expert", "helper"), None),
            P(("expert", "helper"), None, None),
            P(("expert", "helper"), None),
        ),
        check_vma=False,
    )
```

```python
import jax
import jax.numpy as jnp
from jax import lax
from jax.sharding import PartitionSpec as P

AXES = ("expert", "helper")


def lower_ones(samples):
    index = jnp.arange(samples, dtype=jnp.int32)
    return (index[:, None] > index[None, :]).astype(jnp.bfloat16)


def ranks_of(route_ids, groups):
    samples = route_ids.shape[0]
    onehot = (route_ids[:, None] == jnp.arange(groups, dtype=jnp.int32)[None, :]).astype(
        jnp.bfloat16
    )
    before = jnp.dot(lower_ones(samples), onehot, preferred_element_type=jnp.float32)
    return jnp.sum(before * onehot.astype(jnp.float32), axis=1).astype(jnp.int32)


def forward_pass(inputs, weight, bias_row):
    slot_count, depth, feature_dim = inputs.shape
    product = jnp.dot(
        inputs.reshape(slot_count * depth, feature_dim), weight, preferred_element_type=jnp.float32
    ).reshape(slot_count, depth, feature_dim)
    preact = product[:, 0] + bias_row[None, :]
    directed = product[:, 1:]
    slopes = jax.nn.sigmoid(preact)
    values = jax.nn.softplus(preact).astype(jnp.bfloat16)
    carried = (slopes[:, None] * directed).astype(jnp.bfloat16)
    return jnp.concatenate([values[:, None], carried], axis=1), slopes, directed


def backward_pass(inputs, slopes, directed, cotangent):
    slot_count, depth, feature_dim = inputs.shape
    cot_float = cotangent.astype(jnp.float32)
    grad_pre = cot_float[:, 0] * slopes + jnp.sum(cot_float[:, 1:] * directed, axis=1) * slopes * (
        1.0 - slopes
    )
    grad_dir = (cot_float[:, 1:] * slopes[:, None]).astype(jnp.bfloat16)
    gradients = jnp.concatenate([grad_pre.astype(jnp.bfloat16)[:, None], grad_dir], axis=1)
    weight_grad = lax.dot_general(
        inputs.reshape(slot_count * depth, feature_dim),
        gradients.reshape(slot_count * depth, feature_dim),
        (((0,), (0,)), ((), ())),
        preferred_element_type=jnp.float32,
    )
    return weight_grad, jnp.sum(grad_pre, axis=0)


def body(
    route_ids, hot_expert, features, tangents, expert_weight, expert_bias, cot_value, cot_tangent
):
    n_expert = lax.axis_size("expert")
    n_helper = lax.axis_size("helper")
    groups = n_expert * n_helper
    samples = route_ids.shape[0]
    feature_dim = features.shape[1]
    cap = 2 * samples // groups
    me = lax.axis_index("expert") * n_helper + lax.axis_index("helper")
    is_hot = me == hot_expert[0]
    weight = expert_weight[0]
    bias_row = expert_bias[0]

    rank = ranks_of(route_ids, groups)
    slot = route_ids * cap + rank
    main = rank < cap
    dispatch = (
        (slot[None, :] == jnp.arange(groups * cap, dtype=jnp.int32)[:, None]) & main[None, :]
    ).astype(jnp.bfloat16)
    extra = jnp.logical_not(main)

    def place(stacked):
        return jnp.einsum(
            "sp,apd->sad", dispatch, stacked, preferred_element_type=jnp.float32
        ).astype(jnp.bfloat16).reshape(groups, cap * 4, feature_dim)

    def transfer(stacked):
        return lax.all_to_all(stacked, AXES, 0, 0, tiled=True).reshape(groups * cap, 4, feature_dim)

    inputs_local = jnp.concatenate([features[None], tangents], axis=0)
    cot_local = jnp.concatenate([cot_value[None], cot_tangent], axis=0)
    stacked = jnp.concatenate([inputs_local, cot_local], axis=0)
    extra_rows = jnp.einsum(
        "p,apd->ad", extra.astype(jnp.bfloat16), stacked, preferred_element_type=jnp.float32
    ).astype(jnp.bfloat16)
    gathered = lax.all_gather(extra_rows, AXES, axis=0, tiled=False)
    gathered = jnp.where(is_hot, gathered, jnp.zeros_like(gathered))

    inputs = transfer(place(inputs_local))
    inputs, cot_send = lax.optimization_barrier((inputs, place(cot_local)))
    cotangent = transfer(cot_send)

    results, slopes, directed = forward_pass(inputs, weight, bias_row)
    extra_results, extra_slopes, extra_directed = forward_pass(gathered[:, :4], weight, bias_row)
    back = results.reshape(groups, cap * 4, feature_dim)
    back, extra_results, slopes, directed, extra_slopes, extra_directed, cotangent = (
        lax.optimization_barrier(
            (back, extra_results, slopes, directed, extra_slopes, extra_directed, cotangent)
        )
    )
    returned = lax.all_to_all(back, AXES, 0, 0, tiled=True).reshape(groups * cap, 4, feature_dim)
    extra_returned = lax.all_to_all(extra_results, AXES, 0, 0, tiled=True)

    weight_grad, bias_grad = backward_pass(inputs, slopes, directed, cotangent)
    extra_wg, extra_bg = backward_pass(gathered[:, :4], extra_slopes, extra_directed, gathered[:, 4:])

    extra_back = lax.dynamic_index_in_dim(extra_returned, hot_expert[0], axis=0, keepdims=False)
    combined = jnp.einsum(
        "sp,sad->apd", dispatch, returned, preferred_element_type=jnp.float32
    ).astype(jnp.bfloat16)
    outputs = jnp.where(extra[None, :, None], extra_back[:, None, :], combined)
    grad_weight = (weight_grad + extra_wg).astype(jnp.bfloat16)[None]
    grad_bias = (bias_grad + extra_bg)[None]
    return (outputs[0], outputs[1:], grad_weight, grad_bias)


def solution(mesh):
    return jax.shard_map(
        body,
        mesh=mesh,
        in_specs=(
            P(("expert", "helper")),
            P(),
            P(("expert", "helper"), None),
            P(None, ("expert", "helper"), None),
            P(("expert", "helper"), None, None),
            P(("expert", "helper"), None),
            P(("expert", "helper"), None),
            P(None, ("expert", "helper"), None),
        ),
        out_specs=(
            P(("expert", "helper"), None),
            P(None, ("expert", "helper"), None),
            P(("expert", "helper"), None, None),
            P(("expert", "helper"), None),
        ),
        check_vma=False,
    )
```

```python
import jax
import jax.numpy as jnp
from jax import lax
from jax.sharding import PartitionSpec as P

AXES = ("expert", "helper")


def lower_ones(samples):
    index = jnp.arange(samples, dtype=jnp.int32)
    return (index[:, None] > index[None, :]).astype(jnp.bfloat16)


def ranks_of(route_ids, groups):
    samples = route_ids.shape[0]
    onehot = (route_ids[:, None] == jnp.arange(groups, dtype=jnp.int32)[None, :]).astype(
        jnp.bfloat16
    )
    before = jnp.dot(lower_ones(samples), onehot, preferred_element_type=jnp.float32)
    return jnp.sum(before * onehot.astype(jnp.float32), axis=1).astype(jnp.int32)


def forward_pass(inputs, weight, bias_row):
    slot_count, depth, feature_dim = inputs.shape
    product = jnp.dot(
        inputs.reshape(slot_count * depth, feature_dim), weight, preferred_element_type=jnp.float32
    ).reshape(slot_count, depth, feature_dim)
    preact = product[:, 0] + bias_row[None, :]
    directed = product[:, 1:]
    slopes = jax.nn.sigmoid(preact)
    values = jax.nn.softplus(preact).astype(jnp.bfloat16)
    carried = (slopes[:, None] * directed).astype(jnp.bfloat16)
    return jnp.concatenate([values[:, None], carried], axis=1), slopes, directed


def backward_pass(inputs, slopes, directed, cotangent):
    slot_count, depth, feature_dim = inputs.shape
    cot_float = cotangent.astype(jnp.float32)
    grad_pre = cot_float[:, 0] * slopes + jnp.sum(cot_float[:, 1:] * directed, axis=1) * slopes * (
        1.0 - slopes
    )
    grad_dir = (cot_float[:, 1:] * slopes[:, None]).astype(jnp.bfloat16)
    gradients = jnp.concatenate([grad_pre.astype(jnp.bfloat16)[:, None], grad_dir], axis=1)
    weight_grad = lax.dot_general(
        inputs.reshape(slot_count * depth, feature_dim),
        gradients.reshape(slot_count * depth, feature_dim),
        (((0,), (0,)), ((), ())),
        preferred_element_type=jnp.float32,
    )
    return weight_grad, jnp.sum(grad_pre, axis=0)


def body(
    route_ids, hot_expert, features, tangents, expert_weight, expert_bias, cot_value, cot_tangent
):
    n_expert = lax.axis_size("expert")
    n_helper = lax.axis_size("helper")
    groups = n_expert * n_helper
    samples = route_ids.shape[0]
    feature_dim = features.shape[1]
    cap = 2 * samples // groups
    me = lax.axis_index("expert") * n_helper + lax.axis_index("helper")
    is_hot = me == hot_expert[0]
    weight = expert_weight[0]
    bias_row = expert_bias[0]

    rank = ranks_of(route_ids, groups)
    slot = route_ids * cap + rank
    main = rank < cap
    dispatch = (
        (slot[None, :] == jnp.arange(groups * cap, dtype=jnp.int32)[:, None]) & main[None, :]
    ).astype(jnp.bfloat16)
    extra = jnp.logical_not(main)

    def place(stacked):
        return jnp.einsum(
            "sp,apd->sad", dispatch, stacked, preferred_element_type=jnp.float32
        ).astype(jnp.bfloat16).reshape(groups, cap * 4, feature_dim)

    inputs_local = jnp.concatenate([features[None], tangents], axis=0)
    cot_local = jnp.concatenate([cot_value[None], cot_tangent], axis=0)
    stacked = jnp.concatenate([inputs_local, cot_local], axis=0)
    extra_rows = jnp.einsum(
        "p,apd->ad", extra.astype(jnp.bfloat16), stacked, preferred_element_type=jnp.float32
    ).astype(jnp.bfloat16)
    gathered = lax.all_gather(extra_rows, AXES, axis=0, tiled=False)
    gathered = jnp.where(is_hot, gathered, jnp.zeros_like(gathered))

    received = lax.all_to_all(place(inputs_local), AXES, 0, 0, tiled=True)
    received, cot_send = lax.optimization_barrier((received, place(cot_local)))
    cot_received = lax.all_to_all(cot_send, AXES, 0, 0, tiled=True)
    inputs = received.reshape(groups * cap, 4, feature_dim)

    results, slopes, directed = forward_pass(inputs, weight, bias_row)
    extra_results, extra_slopes, extra_directed = forward_pass(gathered[:, :4], weight, bias_row)
    back = jnp.concatenate(
        [results.reshape(groups, cap, 4, feature_dim), extra_results[:, None]], axis=1
    )
    back, slopes, directed, extra_slopes, extra_directed, cot_received = lax.optimization_barrier(
        (back, slopes, directed, extra_slopes, extra_directed, cot_received)
    )
    returned = lax.all_to_all(back, AXES, 0, 0, tiled=True)
    cotangent = cot_received.reshape(groups * cap, 4, feature_dim)

    weight_grad, bias_grad = backward_pass(inputs, slopes, directed, cotangent)
    extra_wg, extra_bg = backward_pass(gathered[:, :4], extra_slopes, extra_directed, gathered[:, 4:])

    extra_back = lax.dynamic_index_in_dim(returned[:, cap], hot_expert[0], axis=0, keepdims=False)
    combined = jnp.einsum(
        "sp,sad->apd",
        dispatch,
        returned[:, :cap].reshape(groups * cap, 4, feature_dim),
        preferred_element_type=jnp.float32,
    ).astype(jnp.bfloat16)
    outputs = jnp.where(extra[None, :, None], extra_back[:, None, :], combined)
    grad_weight = (weight_grad + extra_wg).astype(jnp.bfloat16)[None]
    grad_bias = (bias_grad + extra_bg)[None]
    return (outputs[0], outputs[1:], grad_weight, grad_bias)


def solution(mesh):
    return jax.shard_map(
        body,
        mesh=mesh,
        in_specs=(
            P(("expert", "helper")),
            P(),
            P(("expert", "helper"), None),
            P(None, ("expert", "helper"), None),
            P(("expert", "helper"), None, None),
            P(("expert", "helper"), None),
            P(("expert", "helper"), None),
            P(None, ("expert", "helper"), None),
        ),
        out_specs=(
            P(("expert", "helper"), None),
            P(None, ("expert", "helper"), None),
            P(("expert", "helper"), None, None),
            P(("expert", "helper"), None),
        ),
        check_vma=False,
    )
```

```python
import jax
import jax.numpy as jnp
from jax import lax
from jax.sharding import PartitionSpec as P

AXES = ("expert", "helper")


def lower_ones(samples):
    index = jnp.arange(samples, dtype=jnp.int32)
    return (index[:, None] > index[None, :]).astype(jnp.bfloat16)


def ranks_of(route_ids, groups):
    samples = route_ids.shape[0]
    onehot = (route_ids[:, None] == jnp.arange(groups, dtype=jnp.int32)[None, :]).astype(
        jnp.bfloat16
    )
    before = jnp.dot(lower_ones(samples), onehot, preferred_element_type=jnp.float32)
    return jnp.sum(before * onehot.astype(jnp.float32), axis=1).astype(jnp.int32)


def forward_pass(inputs, weight, bias_row):
    slot_count, depth, feature_dim = inputs.shape
    product = jnp.dot(
        inputs.reshape(slot_count * depth, feature_dim), weight, preferred_element_type=jnp.float32
    ).reshape(slot_count, depth, feature_dim)
    preact = product[:, 0] + bias_row[None, :]
    directed = product[:, 1:]
    slopes = jax.nn.sigmoid(preact)
    values = jax.nn.softplus(preact).astype(jnp.bfloat16)
    carried = (slopes[:, None] * directed).astype(jnp.bfloat16)
    return jnp.concatenate([values[:, None], carried], axis=1), slopes, directed


def backward_pass(inputs, slopes, directed, cotangent):
    slot_count, depth, feature_dim = inputs.shape
    cot_float = cotangent.astype(jnp.float32)
    grad_pre = cot_float[:, 0] * slopes + jnp.sum(cot_float[:, 1:] * directed, axis=1) * slopes * (
        1.0 - slopes
    )
    grad_dir = (cot_float[:, 1:] * slopes[:, None]).astype(jnp.bfloat16)
    gradients = jnp.concatenate([grad_pre.astype(jnp.bfloat16)[:, None], grad_dir], axis=1)
    weight_grad = lax.dot_general(
        inputs.reshape(slot_count * depth, feature_dim),
        gradients.reshape(slot_count * depth, feature_dim),
        (((0,), (0,)), ((), ())),
        preferred_element_type=jnp.float32,
    )
    return weight_grad, jnp.sum(grad_pre, axis=0)


def body(
    route_ids, hot_expert, features, tangents, expert_weight, expert_bias, cot_value, cot_tangent
):
    n_expert = lax.axis_size("expert")
    n_helper = lax.axis_size("helper")
    groups = n_expert * n_helper
    samples = route_ids.shape[0]
    feature_dim = features.shape[1]
    cap = 2 * samples // groups
    me = lax.axis_index("expert") * n_helper + lax.axis_index("helper")
    is_hot = me == hot_expert[0]
    weight = expert_weight[0]
    bias_row = expert_bias[0]

    rank = ranks_of(route_ids, groups)
    slot = route_ids * cap + rank
    main = rank < cap
    dispatch = (
        (slot[None, :] == jnp.arange(groups * cap, dtype=jnp.int32)[:, None]) & main[None, :]
    ).astype(jnp.bfloat16)
    extra = jnp.logical_not(main)

    def place(stacked):
        return jnp.einsum(
            "sp,apd->sad", dispatch, stacked, preferred_element_type=jnp.float32
        ).astype(jnp.bfloat16).reshape(groups, cap, 4, feature_dim)

    inputs_local = jnp.concatenate([features[None], tangents], axis=0)
    cot_local = jnp.concatenate([cot_value[None], cot_tangent], axis=0)
    stacked = jnp.concatenate([inputs_local, cot_local], axis=0)
    extra_rows = jnp.einsum(
        "p,apd->ad", extra.astype(jnp.bfloat16), stacked, preferred_element_type=jnp.float32
    ).astype(jnp.bfloat16)
    gathered = lax.all_gather(extra_rows, AXES, axis=0, tiled=False)
    gathered = jnp.where(is_hot, gathered, jnp.zeros_like(gathered))

    received = lax.all_to_all(place(inputs_local), AXES, 0, 0, tiled=True)
    received, cot_send = lax.optimization_barrier((received, place(cot_local)))
    cot_received = lax.all_to_all(cot_send, AXES, 0, 0, tiled=True)
    inputs = received.reshape(groups * cap, 4, feature_dim)

    results, slopes, directed = forward_pass(inputs, weight, bias_row)
    extra_results, extra_slopes, extra_directed = forward_pass(gathered[:, :4], weight, bias_row)
    back = jnp.concatenate(
        [results.reshape(groups, cap, 4, feature_dim), extra_results[:, None]], axis=1
    )
    back, slopes, directed, extra_slopes, extra_directed, cot_received = lax.optimization_barrier(
        (back, slopes, directed, extra_slopes, extra_directed, cot_received)
    )
    returned = lax.all_to_all(back, AXES, 0, 0, tiled=True)
    cotangent = cot_received.reshape(groups * cap, 4, feature_dim)

    weight_grad, bias_grad = backward_pass(inputs, slopes, directed, cotangent)
    extra_wg, extra_bg = backward_pass(gathered[:, :4], extra_slopes, extra_directed, gathered[:, 4:])

    extra_back = lax.dynamic_index_in_dim(returned[:, cap], hot_expert[0], axis=0, keepdims=False)
    combined = jnp.einsum(
        "sp,sad->apd",
        dispatch,
        returned[:, :cap].reshape(groups * cap, 4, feature_dim),
        preferred_element_type=jnp.float32,
    ).astype(jnp.bfloat16)
    outputs = jnp.where(extra[None, :, None], extra_back[:, None, :], combined)
    grad_weight = (weight_grad + extra_wg).astype(jnp.bfloat16)[None]
    grad_bias = (bias_grad + extra_bg)[None]
    return (outputs[0], outputs[1:], grad_weight, grad_bias)


def solution(mesh):
    return jax.shard_map(
        body,
        mesh=mesh,
        in_specs=(
            P(("expert", "helper")),
            P(),
            P(("expert", "helper"), None),
            P(None, ("expert", "helper"), None),
            P(("expert", "helper"), None, None),
            P(("expert", "helper"), None),
            P(("expert", "helper"), None),
            P(None, ("expert", "helper"), None),
        ),
        out_specs=(
            P(("expert", "helper"), None),
            P(None, ("expert", "helper"), None),
            P(("expert", "helper"), None, None),
            P(("expert", "helper"), None),
        ),
        check_vma=False,
    )
```

```python
import jax
import jax.numpy as jnp
from jax import lax
from jax.sharding import PartitionSpec as P

AXES = ("expert", "helper")


def lower_ones(samples):
    index = jnp.arange(samples, dtype=jnp.int32)
    return (index[:, None] > index[None, :]).astype(jnp.bfloat16)


def ranks_of(route_ids, groups):
    samples = route_ids.shape[0]
    onehot = (route_ids[:, None] == jnp.arange(groups, dtype=jnp.int32)[None, :]).astype(
        jnp.bfloat16
    )
    before = jnp.dot(lower_ones(samples), onehot, preferred_element_type=jnp.float32)
    return jnp.sum(before * onehot.astype(jnp.float32), axis=1).astype(jnp.int32)


def forward_pass(inputs, weight, bias_row):
    slot_count, depth, feature_dim = inputs.shape
    product = jnp.dot(
        inputs.reshape(slot_count * depth, feature_dim), weight, preferred_element_type=jnp.float32
    ).reshape(slot_count, depth, feature_dim)
    preact = product[:, 0] + bias_row[None, :]
    directed = product[:, 1:]
    slopes = jax.nn.sigmoid(preact)
    values = jax.nn.softplus(preact).astype(jnp.bfloat16)
    carried = (slopes[:, None] * directed).astype(jnp.bfloat16)
    return jnp.concatenate([values[:, None], carried], axis=1), slopes, directed


def backward_pass(inputs, slopes, directed, cotangent):
    slot_count, depth, feature_dim = inputs.shape
    cot_float = cotangent.astype(jnp.float32)
    grad_pre = cot_float[:, 0] * slopes + jnp.sum(cot_float[:, 1:] * directed, axis=1) * slopes * (
        1.0 - slopes
    )
    grad_dir = (cot_float[:, 1:] * slopes[:, None]).astype(jnp.bfloat16)
    gradients = jnp.concatenate([grad_pre.astype(jnp.bfloat16)[:, None], grad_dir], axis=1)
    weight_grad = lax.dot_general(
        inputs.reshape(slot_count * depth, feature_dim),
        gradients.reshape(slot_count * depth, feature_dim),
        (((0,), (0,)), ((), ())),
        preferred_element_type=jnp.float32,
    )
    return weight_grad, jnp.sum(grad_pre, axis=0)


def body(
    route_ids, hot_expert, features, tangents, expert_weight, expert_bias, cot_value, cot_tangent
):
    n_expert = lax.axis_size("expert")
    n_helper = lax.axis_size("helper")
    groups = n_expert * n_helper
    samples = route_ids.shape[0]
    feature_dim = features.shape[1]
    cap = 2 * samples // groups
    me = lax.axis_index("expert") * n_helper + lax.axis_index("helper")
    is_hot = me == hot_expert[0]
    weight = expert_weight[0]
    bias_row = expert_bias[0]

    rank = ranks_of(route_ids, groups)
    slot = route_ids * cap + rank
    main = rank < cap
    dispatch = (
        (slot[None, :] == jnp.arange(groups * cap, dtype=jnp.int32)[:, None]) & main[None, :]
    ).astype(jnp.bfloat16)
    extra = jnp.logical_not(main)

    def place(stacked):
        return jnp.einsum(
            "sp,apd->sad", dispatch, stacked, preferred_element_type=jnp.float32
        ).astype(jnp.bfloat16).reshape(groups, cap, 4, feature_dim)

    inputs_local = jnp.concatenate([features[None], tangents], axis=0)
    cot_local = jnp.concatenate([cot_value[None], cot_tangent], axis=0)
    stacked = jnp.concatenate([inputs_local, cot_local], axis=0)
    extra_rows = jnp.einsum(
        "p,apd->ad", extra.astype(jnp.bfloat16), stacked, preferred_element_type=jnp.float32
    ).astype(jnp.bfloat16)
    gathered = lax.all_gather(extra_rows, AXES, axis=0, tiled=False)
    gathered = jnp.where(is_hot, gathered, jnp.zeros_like(gathered))

    received = lax.all_to_all(place(inputs_local), AXES, 0, 0, tiled=True)
    received, cot_send = lax.optimization_barrier((received, place(cot_local)))
    cot_received = lax.all_to_all(cot_send, AXES, 0, 0, tiled=True)
    inputs = received.reshape(groups * cap, 4, feature_dim)

    results, slopes, directed = forward_pass(inputs, weight, bias_row)
    extra_results, extra_slopes, extra_directed = forward_pass(gathered[:, :4], weight, bias_row)
    back = jnp.concatenate(
        [results.reshape(groups, cap, 4, feature_dim), extra_results[:, None]], axis=1
    )
    back, slopes, directed, extra_slopes, extra_directed, cot_received = lax.optimization_barrier(
        (back, slopes, directed, extra_slopes, extra_directed, cot_received)
    )
    returned = lax.all_to_all(back, AXES, 0, 0, tiled=True)
    cotangent = cot_received.reshape(groups * cap, 4, feature_dim)

    weight_grad, bias_grad = backward_pass(inputs, slopes, directed, cotangent)
    extra_wg, extra_bg = backward_pass(gathered[:, :4], extra_slopes, extra_directed, gathered[:, 4:])

    slot3 = jnp.where(main, route_ids * (cap + 1) + rank, hot_expert[0] * (cap + 1) + cap)
    collect = (slot3[None, :] == jnp.arange(groups * (cap + 1), dtype=jnp.int32)[:, None]).astype(
        jnp.bfloat16
    )
    outputs = jnp.einsum(
        "sp,sad->apd",
        collect,
        returned.reshape(groups * (cap + 1), 4, feature_dim),
        preferred_element_type=jnp.float32,
    ).astype(jnp.bfloat16)
    grad_weight = (weight_grad + extra_wg).astype(jnp.bfloat16)[None]
    grad_bias = (bias_grad + extra_bg)[None]
    return (outputs[0], outputs[1:], grad_weight, grad_bias)


def solution(mesh):
    return jax.shard_map(
        body,
        mesh=mesh,
        in_specs=(
            P(("expert", "helper")),
            P(),
            P(("expert", "helper"), None),
            P(None, ("expert", "helper"), None),
            P(("expert", "helper"), None, None),
            P(("expert", "helper"), None),
            P(("expert", "helper"), None),
            P(None, ("expert", "helper"), None),
        ),
        out_specs=(
            P(("expert", "helper"), None),
            P(None, ("expert", "helper"), None),
            P(("expert", "helper"), None, None),
            P(("expert", "helper"), None),
        ),
        check_vma=False,
    )
```
